256 devices in a mesh: tile: 32 (over x, z), atom: 8 (over y, core).
Axes of the slice: x: 4, y: 4, z: 8, core: 2. Of those that a mesh axis runs over, the one named last changes fastest.
Arguments:
- images: float32 [1024, 1024], P(('tile', 'atom')), may hold values from -6 to 6
- active: int32 [1024, 2], P(('tile', 'atom')), may hold values from 0 to 7, all different within a row; in each aligned block of 4 rows (0 to 3, 4 to 7, ...) at most 2 rows name the same one
- dictionary: float32 [8, 32, 1024], P('atom', 'tile'), may hold values from -6 to 6
Outputs:
- reconstruction: float32 [1024, 1024], P(('tile', 'atom'))
- new_dictionary: float32 [8, 32, 1024], P('atom', 'tile')
The draws below stay inside these ranges and needn't reach their ends.
Inputs may be any that keep to these rules, and one draw needn't show every extreme that they name: `active`: each tile names 2 different atom blocks. Among the 4 tiles of one device no block is named by more than 2 tiles, and on some devices one block is named by exactly 2. Every block is named by some tile.
All inputs are finite; a program needn't handle non-finite values.
Results may differ from the reference program's by a relative error of at most 0.0001.
Values sent between devices are 32-bit elements; how exact they have to be, the bound alone decides.
No kernel may reach another device: no remote copies, remote signals or barrier semaphores. Data moves between devices by JAX's collectives and lax.ppermute only.
A program may use at most 128 MiB of HBM per device.

```python
import math
import jax
import jax.numpy as jnp
import numpy as np
from jax import lax

SIDE = 32
PIX = 1024
BLK = 32
NBLK = 8
ACT = 2
TILE_DEV = 4
TILES = 1024
MOST = 2
ITERS = 2
ROUNDS = 1


def steps_of(own_key, extent, pieces, low, top_value):
    def one(position, blocks):
        heights = jax.random.uniform(jax.random.fold_in(jax.random.fold_in(own_key, 6), position), (blocks,), jnp.float32, low / len(pieces), top_value / len(pieces))
        return jnp.repeat(jnp.exp(heights), extent[position] // blocks).reshape((-1,) + (1,) * (len(extent) - position - 1))

    loudness = one(*pieces[0])
    for cut in pieces[1:]:
        loudness = loudness * one(*cut)
    return loudness


def shared_out(stream_key, own, number, rows, amount, top, reach, slope):
    sequence = jax.random.permutation(stream_key, amount)
    heavy_load, common = load_shares(amount, rows * top, reach, slope, True), load_shares(amount, rows * top, reach, slope, False)
    places = jnp.arange(amount)

    def named(tallies, turn):
        used = int((tallies > 0).sum())
        fixed = max(1, used // 4)
        shifted = fixed + (places - fixed + turn * (used - fixed)) % max(1, amount - fixed)
        return jnp.zeros((amount,), jnp.int32).at[sequence[jnp.where(places < fixed, places, shifted)]].set(jnp.asarray(tallies, jnp.int32))

    tallies = jnp.where(number % 4 == 0, named(heavy_load, number // 4), named(common, number - number // 4 - 1))
    mixed = jax.random.permutation(jax.random.fold_in(own, 3), amount)
    donor, receiver = mixed[0:amount // 2 * 2:2], mixed[1:amount // 2 * 2:2]
    room = jnp.minimum(tallies[donor] - 1, reach - tallies[receiver]) // 2
    room = jnp.where((donor == sequence[0]) | (receiver == sequence[0]) | (tallies[receiver] == 0), 0, jnp.maximum(room, 0))
    shifted = jax.random.randint(jax.random.fold_in(own, 4), (amount // 2,), 0, 1 << 20) % (room + 1)
    tallies = tallies.at[donor].add(-shifted).at[receiver].add(shifted)
    items = jnp.searchsorted(jnp.cumsum(tallies), jnp.arange(rows * top), side="right").astype(jnp.int32)
    listing = items.reshape(top, rows).T
    listing = listing[jax.random.permutation(jax.random.fold_in(own, 1), rows)]
    turn = jax.random.randint(jax.random.fold_in(own, 2), (rows, 1), 0, top)
    return jnp.take_along_axis(listing, (jnp.arange(top)[None, :] + turn) % top, axis=1)


def load_shares(amount, total, most, skew, full):
    weights = [(1 << 20) // math.isqrt(standing ** skew) + 1 for standing in range(1, amount + 1)]
    largest = most if full else min(most, max(-(-total // amount), total * weights[0] // sum(weights)))
    least = 1 if total - largest >= amount - 1 else 0
    holding, surplus = [largest] + [least] * (amount - 1), total - largest - least * (amount - 1)
    while surplus > 0:
        candidates = [i for i in range(1, amount) if holding[i] < largest] or [i for i in range(1, amount) if holding[i] < most]
        mass, remaining = sum([weights[i] for i in candidates]), surplus
        for i in candidates:
            more = min(most - holding[i], max(1, remaining * weights[i] // mass), surplus)
            holding[i] = holding[i] + more
            surplus = surplus - more
    return np.array(holding)


def centred(own_key, extent, width, most, shards=(), kind=jnp.bfloat16):
    gain = steps_of(own_key, extent, shards, -0.22, 0.18) if shards else 1.0
    values = jax.random.normal(own_key, extent, jnp.float32) * width * gain
    return jnp.minimum(jnp.maximum(values, -most), most).astype(kind)


def setup_inputs(seed: int = 0) -> dict:
    key_list = jax.random.split(jax.random.key(seed), 4)
    images = centred(key_list[0], (TILES, PIX), 1.0, 6.0, ((0, 256),), jnp.float32)
    active_keys = jax.random.split(jax.random.fold_in(key_list[1], 1), TILES // TILE_DEV)
    active_turns = jax.random.permutation(jax.random.fold_in(key_list[1], 3), TILES // TILE_DEV)
    active = jax.vmap(lambda own, number: shared_out(jax.random.fold_in(key_list[1], 2), own, number, TILE_DEV, NBLK, ACT, MOST, 2))(active_keys, active_turns).reshape((TILES, ACT))
    dictionary = centred(key_list[2], (NBLK, BLK, PIX), 1.0, 6.0, ((0, 8), (1, 32)), jnp.float32)
    return {"images": images, "active": active, "dictionary": dictionary}


shrink_scale = 0.5
step_ratio = 0.5
epsilon = 1e-06

def momentum_weights(count):
    weights = []
    current = 1.0
    for sweep in range(count):
        following = (1.0 + math.sqrt(1.0 + 4.0 * current * current)) / 2.0
        weights.append((current - 1.0) / following)
        current = following
    return weights

def unit_rows(values):
    return values / jnp.sqrt(lax.optimization_barrier(jnp.mean(values * values, axis=-1, keepdims=True)) + epsilon)

def spectrum(values):
    shaped = values.reshape(values.shape[:-1] + (SIDE, SIDE))
    return jnp.fft.fft2(shaped)

def spatial(spectra):
    real_part = jnp.real(jnp.fft.ifft2(spectra))
    return real_part.reshape(real_part.shape[:-2] + (PIX,))

def reference(images, active, dictionary):
    atoms = unit_rows(dictionary)
    image_spec = spectrum(images)
    codes = jnp.zeros((TILES, ACT, BLK, PIX), jnp.float32)
    member = (active[:, :, None] == jnp.arange(NBLK, dtype=jnp.int32)[None, None, :]).astype(jnp.float32)
    weights = momentum_weights(ITERS)
    recon = jnp.zeros((TILES, PIX), jnp.float32)
    for round_index in range(ROUNDS):
        chosen = spectrum(atoms)[active]
        power = jnp.real(chosen * jnp.conj(chosen))
        bound = lax.optimization_barrier(jnp.max(lax.optimization_barrier(jnp.sum(power, axis=(1, 2))), axis=(1, 2))) + epsilon
        rate = (1.0 / bound)[:, None, None, None]
        limit = rate * (shrink_scale * SIDE)
        prior = codes
        guess = codes
        for sweep in range(ITERS):
            residual_spec = lax.optimization_barrier(jnp.sum(chosen * spectrum(guess), axis=(1, 2))) - image_spec
            gradient = spatial(jnp.conj(chosen) * residual_spec[:, None, None])
            moved = guess - rate * gradient
            fresh = moved - jnp.clip(moved, -limit, limit)
            guess = fresh + weights[sweep] * (fresh - prior)
            prior = fresh
        codes = prior
        code_spec = spectrum(codes)
        recon_spec = lax.optimization_barrier(jnp.sum(chosen * code_spec, axis=(1, 2)))
        recon = spatial(recon_spec)
        residual_spec = recon_spec - image_spec
        slot_terms = jnp.conj(code_spec) * residual_spec[:, None, None]
        grad_real = jnp.einsum('tab,taksq->bksq', member, jnp.real(slot_terms))
        grad_imag = jnp.einsum('tab,taksq->bksq', member, jnp.imag(slot_terms))
        atom_grad = spatial(lax.complex(grad_real, grad_imag))
        scale = jnp.sqrt(lax.optimization_barrier(jnp.mean(atom_grad * atom_grad, axis=-1, keepdims=True)) + epsilon)
        atoms = unit_rows(atoms - step_ratio * atom_grad / scale)
    return (recon, atoms)
```

```python
import math

import numpy as np
import jax
import jax.numpy as jnp
from jax import lax
from jax.sharding import PartitionSpec as P

SIDE = 32
BLK = 32
NBLK = 8
ACT = 2
ITERS = 2

shrink_scale = 0.5
step_ratio = 0.5
epsilon = 1e-06
highest = lax.Precision.HIGHEST

HALF = SIDE // 2 + 1
USED = SIDE * HALF
PART = 640


def momentum_weights(count):
    weights = []
    current = 1.0
    for sweep in range(count):
        following = (1.0 + math.sqrt(1.0 + 4.0 * current * current)) / 2.0
        weights.append((current - 1.0) / following)
        current = following
    return weights


def unit_rows(values):
    return values / jnp.sqrt(jnp.mean(values * values, axis=-1, keepdims=True) + epsilon)


def half_table():
    side = np.arange(SIDE)
    phase = (side[:, None, None, None] * side[None, None, :, None]
             + side[None, :, None, None] * np.arange(HALF)[None, None, None, :]) % SIDE
    angle = phase * (2.0 * np.pi / SIDE)
    table = np.zeros((SIDE * SIDE, 2 * PART), np.float32)
    table[:, :USED] = np.cos(angle).reshape(SIDE * SIDE, USED)
    table[:, PART:PART + USED] = -np.sin(angle).reshape(SIDE * SIDE, USED)
    column = np.arange(HALF)
    pair = np.where((column == 0) | (column == SIDE // 2), 1.0, 2.0) / (SIDE * SIDE)
    weight = np.zeros((2 * PART,), np.float32)
    weight[:USED] = np.tile(pair, SIDE)
    weight[PART:PART + USED] = np.tile(pair, SIDE)
    return table, weight


def forward(values, table):
    return jnp.dot(values, table, precision=highest, preferred_element_type=jnp.float32)


def inverse(spectra, table, weight):
    return lax.dot_general(
        spectra * weight, table, (((spectra.ndim - 1,), (1,)), ((), ())),
        precision=highest, preferred_element_type=jnp.float32,
    )


def parts(packed):
    return (packed[..., :PART], packed[..., PART:])


def conj_times(first, second):
    first_real, first_imag = parts(first)
    second_real, second_imag = parts(second)
    real_part = first_real * second_real + first_imag * second_imag
    imag_part = first_real * second_imag - first_imag * second_real
    return jnp.concatenate([real_part, imag_part], axis=-1)


def product_sum(atom_spec, code_spec):
    atom_real, atom_imag = parts(atom_spec)
    code_real, code_imag = parts(code_spec)
    real_sum = jnp.sum(atom_real * code_real - atom_imag * code_imag, axis=1)
    imag_sum = jnp.sum(atom_real * code_imag + atom_imag * code_real, axis=1)
    return jnp.concatenate([real_sum, imag_sum], axis=-1)


def on_device(images, active, dictionary):
    tiles_here, pixels = images.shape
    tile_count = lax.axis_size("tile")
    atom_count = lax.axis_size("atom")
    table_host, weight_host = half_table()
    table = jnp.asarray(table_host)
    weight = jnp.asarray(weight_host)
    width = table.shape[1]

    own = unit_rows(dictionary.reshape(1, pixels))
    step = lax.all_to_all(jnp.broadcast_to(own[None], (tile_count, 1, pixels)), "tile", 0, 0, tiled=True)
    every = lax.all_to_all(
        jnp.broadcast_to(step[None], (atom_count, tile_count, 1, pixels)), "atom", 0, 0, tiled=True
    )
    every = every.reshape(atom_count, tile_count * pixels)

    image_spec = forward(images, table)
    slot_count = tiles_here * ACT
    flat_ids = active.reshape(slot_count)
    chosen_atoms = jnp.take(every, flat_ids, axis=0).reshape(slot_count * BLK, pixels)
    rows = ACT * BLK
    chosen = forward(chosen_atoms, table).reshape(tiles_here, rows, width)
    chosen_real, chosen_imag = parts(chosen)
    power = jnp.sum(chosen_real * chosen_real + chosen_imag * chosen_imag, axis=1)
    bound = jnp.max(power, axis=1) + epsilon
    rate = (1.0 / bound)[:, None, None]
    limit = rate * (shrink_scale * SIDE)
    weights = momentum_weights(ITERS)

    prior = None
    guess = None
    guess_spec = None
    for sweep in range(ITERS):
        if guess is None:
            residual_spec = -image_spec
        else:
            residual_spec = product_sum(chosen, guess_spec) - image_spec
        gradient = inverse(conj_times(chosen, residual_spec[:, None, :]).reshape(tiles_here * rows, width), table, weight)
        gradient = gradient.reshape(tiles_here, rows, pixels)
        if guess is None:
            moved = -(rate * gradient)
        else:
            moved = guess - rate * gradient
        fresh = moved - jnp.clip(moved, -limit, limit)
        if prior is None:
            guess = fresh + weights[sweep] * fresh
        else:
            guess = fresh + weights[sweep] * (fresh - prior)
        prior = fresh
        if sweep + 1 < ITERS:
            guess_spec = forward(guess.reshape(tiles_here * rows, pixels), table).reshape(tiles_here, rows, width)

    code_spec = forward(prior.reshape(tiles_here * rows, pixels), table).reshape(tiles_here, rows, width)
    recon_spec = product_sum(chosen, code_spec)
    recon = inverse(recon_spec, table, weight)
    residual_spec = recon_spec - image_spec
    slot_terms = conj_times(code_spec, residual_spec[:, None, :]).reshape(slot_count, BLK * width)
    member = (jnp.arange(NBLK, dtype=jnp.int32)[:, None] == flat_ids[None, :]).astype(jnp.float32)
    block_spec = jnp.dot(member, slot_terms, precision=highest, preferred_element_type=jnp.float32)
    partial = inverse(block_spec.reshape(NBLK * BLK, width), table, weight).reshape(NBLK, BLK, pixels)

    arrived = jnp.sum(lax.all_to_all(partial, "atom", 0, 0, tiled=True), axis=0)
    arrived = arrived.reshape(tile_count, 1, pixels)
    atom_grad = jnp.sum(lax.all_to_all(arrived, "tile", 0, 0, tiled=True), axis=0)

    scale = jnp.sqrt(jnp.mean(atom_grad * atom_grad, axis=-1, keepdims=True) + epsilon)
    atoms = unit_rows(own - step_ratio * atom_grad / scale)
    return (recon, atoms.reshape(dictionary.shape))


def solution(mesh):
    in_specs = (P(("tile", "atom"), None), P(("tile", "atom"), None), P("atom", "tile", None))
    out_specs = (P(("tile", "atom"), None), P("atom", "tile", None))
    return jax.shard_map(
        on_device, mesh=mesh, in_specs=in_specs, out_specs=out_specs, check_vma=False
    )
```

```python
import math

import numpy as np
import jax
import jax.numpy as jnp
from jax import lax
from jax.sharding import PartitionSpec as P

SIDE = 32
BLK = 32
NBLK = 8
ACT = 2
ITERS = 2

shrink_scale = 0.5
step_ratio = 0.5
epsilon = 1e-06
highest = lax.Precision.HIGHEST
fast = lax.Precision.HIGH

HALF = SIDE // 2 + 1
USED = SIDE * HALF
PART = 640


def momentum_weights(count):
    weights = []
    current = 1.0
    for sweep in range(count):
        following = (1.0 + math.sqrt(1.0 + 4.0 * current * current)) / 2.0
        weights.append((current - 1.0) / following)
        current = following
    return weights


def unit_rows(values):
    return values / jnp.sqrt(jnp.mean(values * values, axis=-1, keepdims=True) + epsilon)


def half_table():
    side = np.arange(SIDE)
    phase = (side[:, None, None, None] * side[None, None, :, None]
             + side[None, :, None, None] * np.arange(HALF)[None, None, None, :]) % SIDE
    angle = phase * (2.0 * np.pi / SIDE)
    table = np.zeros((SIDE * SIDE, 2 * PART), np.float32)
    table[:, :USED] = np.cos(angle).reshape(SIDE * SIDE, USED)
    table[:, PART:PART + USED] = -np.sin(angle).reshape(SIDE * SIDE, USED)
    column = np.arange(HALF)
    pair = np.where((column == 0) | (column == SIDE // 2), 1.0, 2.0) / (SIDE * SIDE)
    weight = np.zeros((2 * PART,), np.float32)
    weight[:USED] = np.tile(pair, SIDE)
    weight[PART:PART + USED] = np.tile(pair, SIDE)
    return table, weight


def forward(values, table):
    return jnp.dot(values, table, precision=fast, preferred_element_type=jnp.float32)


def inverse(spectra, table, weight):
    return lax.dot_general(
        spectra * weight, table, (((spectra.ndim - 1,), (1,)), ((), ())),
        precision=fast, preferred_element_type=jnp.float32,
    )


def parts(packed):
    return (packed[..., :PART], packed[..., PART:])


def conj_times(first, second):
    first_real, first_imag = parts(first)
    second_real, second_imag = parts(second)
    real_part = first_real * second_real + first_imag * second_imag
    imag_part = first_real * second_imag - first_imag * second_real
    return jnp.concatenate([real_part, imag_part], axis=-1)


def product_sum(atom_spec, code_spec):
    atom_real, atom_imag = parts(atom_spec)
    code_real, code_imag = parts(code_spec)
    real_sum = jnp.sum(atom_real * code_real - atom_imag * code_imag, axis=1)
    imag_sum = jnp.sum(atom_real * code_imag + atom_imag * code_real, axis=1)
    return jnp.concatenate([real_sum, imag_sum], axis=-1)


def on_device(images, active, dictionary):
    tiles_here, pixels = images.shape
    tile_count = lax.axis_size("tile")
    atom_count = lax.axis_size("atom")
    table_host, weight_host = half_table()
    table = jnp.asarray(table_host)
    weight = jnp.asarray(weight_host)
    table, weight = lax.optimization_barrier((table, weight))
    width = table.shape[1]

    own = unit_rows(dictionary.reshape(1, pixels))
    step = lax.all_to_all(jnp.broadcast_to(own[None], (tile_count, 1, pixels)), "tile", 0, 0, tiled=True)
    every = lax.all_to_all(
        jnp.broadcast_to(step[None], (atom_count, tile_count, 1, pixels)), "atom", 0, 0, tiled=True
    )
    every = every.reshape(atom_count, tile_count * pixels)

    image_spec = forward(images.reshape(1, tiles_here, pixels), table).reshape(tiles_here, width)
    slot_count = tiles_here * ACT
    flat_ids = active.reshape(slot_count)
    chosen_atoms = jnp.take(every, flat_ids, axis=0).reshape(slot_count * BLK, pixels)
    rows = ACT * BLK
    chosen = forward(chosen_atoms, table).reshape(tiles_here, rows, width)
    chosen_real, chosen_imag = parts(chosen)
    power = jnp.sum(chosen_real * chosen_real + chosen_imag * chosen_imag, axis=1)
    bound = jnp.max(power, axis=1) + epsilon
    rate = (1.0 / bound)[:, None, None]
    limit = rate * (shrink_scale * SIDE)
    weights = momentum_weights(ITERS)

    prior = None
    guess = None
    guess_spec = None
    for sweep in range(ITERS):
        if guess is None:
            residual_spec = -image_spec
        else:
            residual_spec = product_sum(chosen, guess_spec) - image_spec
        gradient = inverse(conj_times(chosen, residual_spec[:, None, :]).reshape(tiles_here * rows, width), table, weight)
        gradient = gradient.reshape(tiles_here, rows, pixels)
        if guess is None:
            moved = -(rate * gradient)
        else:
            moved = guess - rate * gradient
        fresh = moved - jnp.clip(moved, -limit, limit)
        if prior is None:
            guess = fresh + weights[sweep] * fresh
        else:
            guess = fresh + weights[sweep] * (fresh - prior)
        prior = fresh
        if sweep + 1 < ITERS:
            guess_spec = forward(guess.reshape(tiles_here * rows, pixels), table).reshape(tiles_here, rows, width)

    code_spec = forward(prior.reshape(tiles_here * rows, pixels), table).reshape(tiles_here, rows, width)
    recon_spec = product_sum(chosen, code_spec)
    residual_spec = recon_spec - image_spec
    slot_terms = conj_times(code_spec, residual_spec[:, None, :]).reshape(slot_count, BLK * width)
    member = (jnp.arange(NBLK, dtype=jnp.int32)[:, None] == flat_ids[None, :]).astype(jnp.float32)
    block_spec = jnp.dot(member, slot_terms, precision=highest, preferred_element_type=jnp.float32)
    both = inverse(jnp.concatenate([block_spec.reshape(NBLK * BLK, width), recon_spec], axis=0), table, weight)
    partial = both[:NBLK * BLK].reshape(NBLK, BLK, pixels)
    recon = both[NBLK * BLK:]

    arrived = jnp.sum(lax.all_to_all(partial, "atom", 0, 0, tiled=True), axis=0)
    arrived = arrived.reshape(tile_count, 1, pixels)
    atom_grad = jnp.sum(lax.all_to_all(arrived, "tile", 0, 0, tiled=True), axis=0)

    scale = jnp.sqrt(jnp.mean(atom_grad * atom_grad, axis=-1, keepdims=True) + epsilon)
    atoms = unit_rows(own - step_ratio * atom_grad / scale)
    return (recon, atoms.reshape(dictionary.shape))


def solution(mesh):
    in_specs = (P(("tile", "atom"), None), P(("tile", "atom"), None), P("atom", "tile", None))
    out_specs = (P(("tile", "atom"), None), P("atom", "tile", None))
    return jax.shard_map(
        on_device, mesh=mesh, in_specs=in_specs, out_specs=out_specs, check_vma=False
    )
```

```python
import math

import numpy as np
import jax
import jax.numpy as jnp
from jax import lax
from jax.sharding import PartitionSpec as P

SIDE = 32
BLK = 32
NBLK = 8
ACT = 2
ITERS = 2

shrink_scale = 0.5
step_ratio = 0.5
epsilon = 1e-06
highest = lax.Precision.HIGHEST
fast = lax.Precision.HIGH

HALF = SIDE // 2 + 1
USED = SIDE * HALF
PART = 640


def momentum_weights(count):
    weights = []
    current = 1.0
    for sweep in range(count):
        following = (1.0 + math.sqrt(1.0 + 4.0 * current * current)) / 2.0
        weights.append((current - 1.0) / following)
        current = following
    return weights


def unit_rows(values):
    return values / jnp.sqrt(jnp.mean(values * values, axis=-1, keepdims=True) + epsilon)


def half_table():
    side = np.arange(SIDE)
    phase = (side[:, None, None, None] * side[None, None, :, None]
             + side[None, :, None, None] * np.arange(HALF)[None, None, None, :]) % SIDE
    angle = phase * (2.0 * np.pi / SIDE)
    table = np.zeros((SIDE * SIDE, 2 * PART), np.float32)
    table[:, :USED] = np.cos(angle).reshape(SIDE * SIDE, USED)
    table[:, PART:PART + USED] = -np.sin(angle).reshape(SIDE * SIDE, USED)
    column = np.arange(HALF)
    pair = np.where((column == 0) | (column == SIDE // 2), 1.0, 2.0) / (SIDE * SIDE)
    weight = np.zeros((2 * PART,), np.float32)
    weight[:USED] = np.tile(pair, SIDE)
    weight[PART:PART + USED] = np.tile(pair, SIDE)
    return table, weight


def forward(values, table):
    return jnp.dot(values, table, precision=fast, preferred_element_type=jnp.float32)


def inverse(spectra, table, weight):
    return lax.dot_general(
        spectra * weight, table, (((spectra.ndim - 1,), (1,)), ((), ())),
        precision=fast, preferred_element_type=jnp.float32,
    )


def parts(packed):
    return (packed[..., :PART], packed[..., PART:])


def conj_times(first, second):
    first_real, first_imag = parts(first)
    second_real, second_imag = parts(second)
    real_part = first_real * second_real + first_imag * second_imag
    imag_part = first_real * second_imag - first_imag * second_real
    return jnp.concatenate([real_part, imag_part], axis=-1)


def product_sum(atom_spec, code_spec):
    atom_real, atom_imag = parts(atom_spec)
    code_real, code_imag = parts(code_spec)
    real_sum = jnp.sum(atom_real * code_real - atom_imag * code_imag, axis=1)
    imag_sum = jnp.sum(atom_real * code_imag + atom_imag * code_real, axis=1)
    return jnp.concatenate([real_sum, imag_sum], axis=-1)


def on_device(images, active, dictionary):
    tiles_here, pixels = images.shape
    tile_count = lax.axis_size("tile")
    atom_count = lax.axis_size("atom")
    table_host, weight_host = half_table()
    table = jnp.asarray(table_host)
    weight = jnp.asarray(weight_host)
    table, weight = lax.optimization_barrier((table, weight))
    width = table.shape[1]

    own = unit_rows(dictionary.reshape(1, pixels))
    step = lax.all_to_all(jnp.broadcast_to(own[None], (tile_count, 1, pixels)), "tile", 0, 0, tiled=True)
    mine = step.reshape(1, tile_count * pixels)
    place = lax.axis_index("atom")
    core = place % 2
    chips = atom_count // 2
    chip = place // 2
    other = lax.ppermute(mine, "atom", [(i, i ^ 1) for i in range(atom_count)])
    pair = jnp.where(core == 0, jnp.concatenate([mine, other]), jnp.concatenate([other, mine]))
    pieces = [pair]
    for hop in range(1, chips):
        pieces.append(lax.ppermute(pair, "atom", [(i, ((i // 2 + hop) % chips) * 2 + i % 2) for i in range(atom_count)]))
    every = jnp.concatenate(pieces, axis=0)

    image_spec = forward(images.reshape(1, tiles_here, pixels), table).reshape(tiles_here, width)
    slot_count = tiles_here * ACT
    flat_ids = active.reshape(slot_count)
    where_held = ((chip - flat_ids // 2) % chips) * 2 + flat_ids % 2
    chosen_atoms = jnp.take(every, where_held, axis=0).reshape(slot_count * BLK, pixels)
    rows = ACT * BLK
    chosen = forward(chosen_atoms, table).reshape(tiles_here, rows, width)
    chosen_real, chosen_imag = parts(chosen)
    power = jnp.sum(chosen_real * chosen_real + chosen_imag * chosen_imag, axis=1)
    bound = jnp.max(power, axis=1) + epsilon
    rate = (1.0 / bound)[:, None, None]
    limit = rate * (shrink_scale * SIDE)
    weights = momentum_weights(ITERS)

    prior = None
    guess = None
    guess_spec = None
    for sweep in range(ITERS):
        if guess is None:
            residual_spec = -image_spec
        else:
            residual_spec = product_sum(chosen, guess_spec) - image_spec
        gradient = inverse(conj_times(chosen, residual_spec[:, None, :]).reshape(tiles_here * rows, width), table, weight)
        gradient = gradient.reshape(tiles_here, rows, pixels)
        if guess is None:
            moved = -(rate * gradient)
        else:
            moved = guess - rate * gradient
        fresh = moved - jnp.clip(moved, -limit, limit)
        if prior is None:
            guess = fresh + weights[sweep] * fresh
        else:
            guess = fresh + weights[sweep] * (fresh - prior)
        prior = fresh
        if sweep + 1 < ITERS:
            guess_spec = forward(guess.reshape(tiles_here * rows, pixels), table).reshape(tiles_here, rows, width)

    code_spec = forward(prior.reshape(tiles_here * rows, pixels), table).reshape(tiles_here, rows, width)
    recon_spec = product_sum(chosen, code_spec)
    residual_spec = recon_spec - image_spec
    slot_terms = conj_times(code_spec, residual_spec[:, None, :]).reshape(slot_count, BLK * width)
    member = (jnp.arange(NBLK, dtype=jnp.int32)[:, None] == flat_ids[None, :]).astype(jnp.float32)
    block_spec = jnp.dot(member, slot_terms, precision=highest, preferred_element_type=jnp.float32)
    both = inverse(jnp.concatenate([block_spec.reshape(NBLK * BLK, width), recon_spec], axis=0), table, weight)
    partial = both[:NBLK * BLK].reshape(NBLK, BLK, pixels)
    recon = both[NBLK * BLK:]

    paired = partial.reshape(chips, 2, BLK, pixels)
    keep = lax.dynamic_index_in_dim(paired, core, axis=1, keepdims=False)
    give = lax.dynamic_index_in_dim(paired, 1 - core, axis=1, keepdims=False)
    summed = keep + lax.ppermute(give, "atom", [(i, i ^ 1) for i in range(atom_count)])
    arrived = lax.dynamic_index_in_dim(summed, chip, axis=0, keepdims=False)
    for hop in range(1, chips):
        sent = lax.dynamic_index_in_dim(summed, (chip + hop) % chips, axis=0, keepdims=False)
        arrived = arrived + lax.ppermute(sent, "atom", [(i, ((i // 2 + hop) % chips) * 2 + i % 2) for i in range(atom_count)])
    arrived = arrived.reshape(tile_count, 1, pixels)
    atom_grad = jnp.sum(lax.all_to_all(arrived, "tile", 0, 0, tiled=True), axis=0)

    scale = jnp.sqrt(jnp.mean(atom_grad * atom_grad, axis=-1, keepdims=True) + epsilon)
    atoms = unit_rows(own - step_ratio * atom_grad / scale)
    return (recon, atoms.reshape(dictionary.shape))


def solution(mesh):
    in_specs = (P(("tile", "atom"), None), P(("tile", "atom"), None), P("atom", "tile", None))
    out_specs = (P(("tile", "atom"), None), P("atom", "tile", None))
    return jax.shard_map(
        on_device, mesh=mesh, in_specs=in_specs, out_specs=out_specs, check_vma=False
    )
```

```python
import math

import numpy as np
import jax
import jax.numpy as jnp
from jax import lax
from jax.sharding import PartitionSpec as P

SIDE = 32
BLK = 32
NBLK = 8
ACT = 2
ITERS = 2

shrink_scale = 0.5
step_ratio = 0.5
epsilon = 1e-06
highest = lax.Precision.HIGHEST
fast = lax.Precision.HIGH

HALF = SIDE // 2 + 1
USED = SIDE * HALF
PART = 640


def momentum_weights(count):
    weights = []
    current = 1.0
    for sweep in range(count):
        following = (1.0 + math.sqrt(1.0 + 4.0 * current * current)) / 2.0
        weights.append((current - 1.0) / following)
        current = following
    return weights


def unit_rows(values):
    return values / jnp.sqrt(jnp.mean(values * values, axis=-1, keepdims=True) + epsilon)


def half_table():
    side = np.arange(SIDE)
    phase = (side[:, None, None, None] * side[None, None, :, None]
             + side[None, :, None, None] * np.arange(HALF)[None, None, None, :]) % SIDE
    angle = phase * (2.0 * np.pi / SIDE)
    table = np.zeros((SIDE * SIDE, 2 * PART), np.float32)
    table[:, :USED] = np.cos(angle).reshape(SIDE * SIDE, USED)
    table[:, PART:PART + USED] = -np.sin(angle).reshape(SIDE * SIDE, USED)
    column = np.arange(HALF)
    pair = np.where((column == 0) | (column == SIDE // 2), 1.0, 2.0) / (SIDE * SIDE)
    weight = np.zeros((2 * PART,), np.float32)
    weight[:USED] = np.tile(pair, SIDE)
    weight[PART:PART + USED] = np.tile(pair, SIDE)
    return table, weight


def forward(values, table):
    return jnp.dot(values, table, precision=fast, preferred_element_type=jnp.float32)


def inverse(spectra, table, weight):
    return lax.dot_general(
        spectra * weight, table, (((spectra.ndim - 1,), (1,)), ((), ())),
        precision=fast, preferred_element_type=jnp.float32,
    )


def parts(packed):
    return (packed[..., :PART], packed[..., PART:])


def conj_times(first, second):
    first_real, first_imag = parts(first)
    second_real, second_imag = parts(second)
    real_part = first_real * second_real + first_imag * second_imag
    imag_part = first_real * second_imag - first_imag * second_real
    return jnp.concatenate([real_part, imag_part], axis=-1)


def product_sum(atom_spec, code_spec):
    atom_real, atom_imag = parts(atom_spec)
    code_real, code_imag = parts(code_spec)
    real_sum = jnp.sum(atom_real * code_real - atom_imag * code_imag, axis=1)
    imag_sum = jnp.sum(atom_real * code_imag + atom_imag * code_real, axis=1)
    return jnp.concatenate([real_sum, imag_sum], axis=-1)


def on_device(images, active, dictionary):
    tiles_here, pixels = images.shape
    tile_count = lax.axis_size("tile")
    atom_count = lax.axis_size("atom")
    table_host, weight_host = half_table()
    table = jnp.asarray(table_host)
    weight = jnp.asarray(weight_host)
    table, weight = lax.optimization_barrier((table, weight))
    width = table.shape[1]

    raw = dictionary.reshape(1, pixels)
    step = lax.all_to_all(jnp.broadcast_to(raw[None], (tile_count, 1, pixels)), "tile", 0, 0, tiled=True)
    mine = step.reshape(tile_count, pixels)
    own = unit_rows(raw)
    place = lax.axis_index("atom")
    core = place % 2
    chips = atom_count // 2
    chip = place // 2
    other = lax.ppermute(mine, "atom", [(i, i ^ 1) for i in range(atom_count)])
    pair = jnp.concatenate([mine, other])
    pieces = [pair]
    for hop in range(1, chips):
        pieces.append(lax.ppermute(pair, "atom", [(i, ((i // 2 + hop) % chips) * 2 + i % 2) for i in range(atom_count)]))
    every = jnp.concatenate(pieces, axis=0).reshape(atom_count, tile_count * pixels)

    image_spec = forward(images.reshape(1, tiles_here, pixels), table).reshape(tiles_here, width)
    slot_count = tiles_here * ACT
    flat_ids = active.reshape(slot_count)
    where_held = ((chip - flat_ids // 2) % chips) * 2 + (flat_ids % 2 != core).astype(jnp.int32)
    chosen_atoms = unit_rows(jnp.take(every, where_held, axis=0).reshape(slot_count * BLK, pixels))
    rows = ACT * BLK
    chosen = forward(chosen_atoms, table).reshape(tiles_here, rows, width)
    chosen_real, chosen_imag = parts(chosen)
    power = jnp.sum(chosen_real * chosen_real + chosen_imag * chosen_imag, axis=1)
    bound = jnp.max(power, axis=1) + epsilon
    rate = (1.0 / bound)[:, None, None]
    limit = rate * (shrink_scale * SIDE)
    weights = momentum_weights(ITERS)

    prior = None
    guess = None
    guess_spec = None
    for sweep in range(ITERS):
        if guess is None:
            residual_spec = -image_spec
        else:
            residual_spec = product_sum(chosen, guess_spec) - image_spec
        gradient = inverse(conj_times(chosen, residual_spec[:, None, :]).reshape(tiles_here * rows, width), table, weight)
        gradient = gradient.reshape(tiles_here, rows, pixels)
        if guess is None:
            moved = -(rate * gradient)
        else:
            moved = guess - rate * gradient
        fresh = moved - jnp.clip(moved, -limit, limit)
        if prior is None:
            guess = fresh + weights[sweep] * fresh
        else:
            guess = fresh + weights[sweep] * (fresh - prior)
        prior = fresh
        if sweep + 1 < ITERS:
            guess_spec = forward(guess.reshape(tiles_here * rows, pixels), table).reshape(tiles_here, rows, width)

    code_spec = forward(prior.reshape(tiles_here * rows, pixels), table).reshape(tiles_here, rows, width)
    recon_spec = product_sum(chosen, code_spec)
    residual_spec = recon_spec - image_spec
    slot_terms = conj_times(code_spec, residual_spec[:, None, :]).reshape(slot_count, BLK * width)
    member = (jnp.arange(NBLK, dtype=jnp.int32)[:, None] == flat_ids[None, :]).astype(jnp.float32)
    block_spec = jnp.dot(member, slot_terms, precision=highest, preferred_element_type=jnp.float32)
    both = inverse(jnp.concatenate([block_spec.reshape(NBLK * BLK, width), recon_spec], axis=0), table, weight)
    partial = both[:NBLK * BLK].reshape(NBLK, BLK, pixels)
    recon = both[NBLK * BLK:]

    paired = partial.reshape(chips, 2, BLK, pixels)
    keep = lax.dynamic_index_in_dim(paired, core, axis=1, keepdims=False)
    give = lax.dynamic_index_in_dim(paired, 1 - core, axis=1, keepdims=False)
    summed = keep + lax.ppermute(give, "atom", [(i, i ^ 1) for i in range(atom_count)])
    arrived = lax.dynamic_index_in_dim(summed, chip, axis=0, keepdims=False)
    for hop in range(1, chips):
        sent = lax.dynamic_index_in_dim(summed, (chip + hop) % chips, axis=0, keepdims=False)
        arrived = arrived + lax.ppermute(sent, "atom", [(i, ((i // 2 + hop) % chips) * 2 + i % 2) for i in range(atom_count)])
    arrived = arrived.reshape(tile_count, 1, pixels)
    atom_grad = jnp.sum(lax.all_to_all(arrived, "tile", 0, 0, tiled=True), axis=0)

    scale = jnp.sqrt(jnp.mean(atom_grad * atom_grad, axis=-1, keepdims=True) + epsilon)
    atoms = unit_rows(own - step_ratio * atom_grad / scale)
    return (recon, atoms.reshape(dictionary.shape))


def solution(mesh):
    in_specs = (P(("tile", "atom"), None), P(("tile", "atom"), None), P("atom", "tile", None))
    out_specs = (P(("tile", "atom"), None), P("atom", "tile", None))
    return jax.shard_map(
        on_device, mesh=mesh, in_specs=in_specs, out_specs=out_specs, check_vma=False
    )
```

```python
import math

import numpy as np
import jax
import jax.numpy as jnp
from jax import lax
from jax.sharding import PartitionSpec as P

SIDE = 32
BLK = 32
NBLK = 8
ACT = 2
ITERS = 2

shrink_scale = 0.5
step_ratio = 0.5
epsilon = 1e-06
highest = lax.Precision.HIGHEST
fast = lax.Precision.HIGH

HALF = SIDE // 2 + 1
USED = SIDE * HALF
PART = 640


def momentum_weights(count):
    weights = []
    current = 1.0
    for sweep in range(count):
        following = (1.0 + math.sqrt(1.0 + 4.0 * current * current)) / 2.0
        weights.append((current - 1.0) / following)
        current = following
    return weights


def unit_rows(values):
    return values / jnp.sqrt(jnp.mean(values * values, axis=-1, keepdims=True) + epsilon)


def half_weight():
    column = np.arange(HALF)
    pair = np.where((column == 0) | (column == SIDE // 2), 1.0, 2.0) / (SIDE * SIDE)
    weight = np.zeros((2 * PART,), np.float32)
    weight[:USED] = np.repeat(pair, SIDE)
    weight[PART:PART + USED] = np.repeat(pair, SIDE)
    return weight


def half_table(salt):
    shape = (SIDE * SIDE, 2 * PART)
    row = lax.broadcasted_iota(jnp.int32, shape, 0)
    column = lax.broadcasted_iota(jnp.int32, shape, 1)
    imag = column >= PART
    spot = jnp.where(imag, column - PART, column)
    quarter = jnp.where(imag, SIDE // 4, 0)
    phase = ((row // SIDE) * (spot % SIDE) + (row % SIDE) * (spot // SIDE) + quarter + salt) % SIDE
    value = jnp.cos(phase.astype(jnp.float32) * (2.0 * math.pi / SIDE))
    return jnp.where(spot < USED, value, 0.0)


def forward(values, table):
    return jnp.dot(values, table, precision=fast, preferred_element_type=jnp.float32)


def inverse(spectra, table, weight):
    return lax.dot_general(
        spectra * weight, table, (((spectra.ndim - 1,), (1,)), ((), ())),
        precision=fast, preferred_element_type=jnp.float32,
    )


def parts(packed):
    return (packed[..., :PART], packed[..., PART:])


def conj_times(first, second):
    first_real, first_imag = parts(first)
    second_real, second_imag = parts(second)
    real_part = first_real * second_real + first_imag * second_imag
    imag_part = first_real * second_imag - first_imag * second_real
    return jnp.concatenate([real_part, imag_part], axis=-1)


def product_sum(atom_spec, code_spec):
    atom_real, atom_imag = parts(atom_spec)
    code_real, code_imag = parts(code_spec)
    real_sum = jnp.sum(atom_real * code_real - atom_imag * code_imag, axis=1)
    imag_sum = jnp.sum(atom_real * code_imag + atom_imag * code_real, axis=1)
    return jnp.concatenate([real_sum, imag_sum], axis=-1)


def on_device(images, active, dictionary):
    tiles_here, pixels = images.shape
    tile_count = lax.axis_size("tile")
    atom_count = lax.axis_size("atom")
    table = lax.optimization_barrier(half_table(lax.axis_index("tile") * SIDE))
    weight = jnp.asarray(half_weight())
    width = table.shape[1]

    raw = dictionary.reshape(1, pixels)
    step = lax.all_to_all(jnp.broadcast_to(raw[None], (tile_count, 1, pixels)), "tile", 0, 0, tiled=True)
    mine = step.reshape(tile_count, pixels)
    own = unit_rows(raw)
    place = lax.axis_index("atom")
    core = place % 2
    chips = atom_count // 2
    chip = place // 2
    other = lax.ppermute(mine, "atom", [(i, i ^ 1) for i in range(atom_count)])
    pair = jnp.concatenate([mine, other])
    pieces = [pair]
    for hop in range(1, chips):
        pieces.append(lax.ppermute(pair, "atom", [(i, ((i // 2 + hop) % chips) * 2 + i % 2) for i in range(atom_count)]))
    every = jnp.concatenate(pieces, axis=0).reshape(atom_count, tile_count * pixels)

    image_spec = forward(images.reshape(1, tiles_here, pixels), table).reshape(tiles_here, width)
    slot_count = tiles_here * ACT
    flat_ids = active.reshape(slot_count)
    where_held = ((chip - flat_ids // 2) % chips) * 2 + (flat_ids % 2 != core).astype(jnp.int32)
    chosen_atoms = unit_rows(jnp.take(every, where_held, axis=0).reshape(slot_count * BLK, pixels))
    rows = ACT * BLK
    chosen = forward(chosen_atoms, table).reshape(tiles_here, rows, width)
    chosen_real, chosen_imag = parts(chosen)
    power = jnp.sum(chosen_real * chosen_real + chosen_imag * chosen_imag, axis=1)
    bound = jnp.max(power, axis=1) + epsilon
    rate = (1.0 / bound)[:, None, None]
    limit = rate * (shrink_scale * SIDE)
    weights = momentum_weights(ITERS)

    prior = None
    guess = None
    guess_spec = None
    for sweep in range(ITERS):
        if guess is None:
            residual_spec = -image_spec
        else:
            residual_spec = product_sum(chosen, guess_spec) - image_spec
        gradient = inverse(conj_times(chosen, residual_spec[:, None, :]).reshape(tiles_here * rows, width), table, weight)
        gradient = gradient.reshape(tiles_here, rows, pixels)
        if guess is None:
            moved = -(rate * gradient)
        else:
            moved = guess - rate * gradient
        fresh = moved - jnp.clip(moved, -limit, limit)
        if prior is None:
            guess = fresh + weights[sweep] * fresh
        else:
            guess = fresh + weights[sweep] * (fresh - prior)
        prior = fresh
        if sweep + 1 < ITERS:
            guess_spec = forward(guess.reshape(tiles_here * rows, pixels), table).reshape(tiles_here, rows, width)

    code_spec = forward(prior.reshape(tiles_here * rows, pixels), table).reshape(tiles_here, rows, width)
    recon_spec = product_sum(chosen, code_spec)
    residual_spec = recon_spec - image_spec
    slot_terms = conj_times(code_spec, residual_spec[:, None, :]).reshape(slot_count, BLK * width)
    member = (jnp.arange(NBLK, dtype=jnp.int32)[:, None] == flat_ids[None, :]).astype(jnp.float32)
    block_spec = jnp.dot(member, slot_terms, precision=highest, preferred_element_type=jnp.float32)
    both = inverse(jnp.concatenate([block_spec.reshape(NBLK * BLK, width), recon_spec], axis=0), table, weight)
    partial = both[:NBLK * BLK].reshape(NBLK, BLK, pixels)
    recon = both[NBLK * BLK:]

    paired = partial.reshape(chips, 2, BLK, pixels)
    keep = lax.dynamic_index_in_dim(paired, core, axis=1, keepdims=False)
    give = lax.dynamic_index_in_dim(paired, 1 - core, axis=1, keepdims=False)
    summed = keep + lax.ppermute(give, "atom", [(i, i ^ 1) for i in range(atom_count)])
    arrived = lax.dynamic_index_in_dim(summed, chip, axis=0, keepdims=False)
    for hop in range(1, chips):
        sent = lax.dynamic_index_in_dim(summed, (chip + hop) % chips, axis=0, keepdims=False)
        arrived = arrived + lax.ppermute(sent, "atom", [(i, ((i // 2 + hop) % chips) * 2 + i % 2) for i in range(atom_count)])
    arrived = arrived.reshape(tile_count, 1, pixels)
    atom_grad = jnp.sum(lax.all_to_all(arrived, "tile", 0, 0, tiled=True), axis=0)

    scale = jnp.sqrt(jnp.mean(atom_grad * atom_grad, axis=-1, keepdims=True) + epsilon)
    atoms = unit_rows(own - step_ratio * atom_grad / scale)
    return (recon, atoms.reshape(dictionary.shape))


def solution(mesh):
    in_specs = (P(("tile", "atom"), None), P(("tile", "atom"), None), P("atom", "tile", None))
    out_specs = (P(("tile", "atom"), None), P("atom", "tile", None))
    return jax.shard_map(
        on_device, mesh=mesh, in_specs=in_specs, out_specs=out_specs, check_vma=False
    )
```

```python
import math

import numpy as np
import jax
import jax.numpy as jnp
from jax import lax
from jax.sharding import PartitionSpec as P

SIDE = 32
BLK = 32
NBLK = 8
ACT = 2
ITERS = 2

shrink_scale = 0.5
step_ratio = 0.5
epsilon = 1e-06
highest = lax.Precision.HIGHEST

HALF = SIDE // 2 + 1
USED = SIDE * HALF
PART = 640


def momentum_weights(count):
    weights = []
    current = 1.0
    for sweep in range(count):
        following = (1.0 + math.sqrt(1.0 + 4.0 * current * current)) / 2.0
        weights.append((current - 1.0) / following)
        current = following
    return weights


def unit_rows(values):
    return values / jnp.sqrt(jnp.mean(values * values, axis=-1, keepdims=True) + epsilon)


def half_table():
    side = np.arange(SIDE)
    phase = (side[:, None, None, None] * side[None, None, :, None]
             + side[None, :, None, None] * np.arange(HALF)[None, None, None, :]) % SIDE
    angle = phase * (2.0 * np.pi / SIDE)
    table = np.zeros((SIDE * SIDE, 2 * PART), np.float32)
    table[:, :USED] = np.cos(angle).reshape(SIDE * SIDE, USED)
    table[:, PART:PART + USED] = -np.sin(angle).reshape(SIDE * SIDE, USED)
    high = table.astype(jnp.bfloat16)
    low = (table - high.astype(np.float32)).astype(jnp.bfloat16)
    column = np.arange(HALF)
    pair = np.where((column == 0) | (column == SIDE // 2), 1.0, 2.0) / (SIDE * SIDE)
    weight = np.zeros((2 * PART,), np.float32)
    weight[:USED] = np.tile(pair, SIDE)
    weight[PART:PART + USED] = np.tile(pair, SIDE)
    return high, low, weight


def halves(values):
    rounded = lax.reduce_precision(values, exponent_bits=8, mantissa_bits=7)
    return rounded.astype(jnp.bfloat16), (values - rounded).astype(jnp.bfloat16)


def three_products(values, table, dims):
    value_high, value_low = halves(values)
    table_high, table_low = table

    def product(first, second):
        return lax.dot_general(first, second, dims, preferred_element_type=jnp.float32)

    return product(value_high, table_high) + product(value_high, table_low) + product(value_low, table_high)


def forward(values, table):
    return three_products(values, table, (((values.ndim - 1,), (0,)), ((), ())))


def inverse(spectra, table, weight):
    return three_products(spectra * weight, table, (((spectra.ndim - 1,), (1,)), ((), ())))


def parts(packed):
    return (packed[..., :PART], packed[..., PART:])


def conj_times(first, second):
    first_real, first_imag = parts(first)
    second_real, second_imag = parts(second)
    real_part = first_real * second_real + first_imag * second_imag
    imag_part = first_real * second_imag - first_imag * second_real
    return jnp.concatenate([real_part, imag_part], axis=-1)


def product_sum(atom_spec, code_spec):
    atom_real, atom_imag = parts(atom_spec)
    code_real, code_imag = parts(code_spec)
    real_sum = jnp.sum(atom_real * code_real - atom_imag * code_imag, axis=1)
    imag_sum = jnp.sum(atom_real * code_imag + atom_imag * code_real, axis=1)
    return jnp.concatenate([real_sum, imag_sum], axis=-1)


def on_device(images, active, dictionary):
    tiles_here, pixels = images.shape
    tile_count = lax.axis_size("tile")
    atom_count = lax.axis_size("atom")
    high_host, low_host, weight_host = half_table()
    table = lax.optimization_barrier((jnp.asarray(high_host), jnp.asarray(low_host)))
    weight = jnp.asarray(weight_host)
    width = weight.shape[0]

    raw = dictionary.reshape(1, pixels)
    step = lax.all_to_all(jnp.broadcast_to(raw[None], (tile_count, 1, pixels)), "tile", 0, 0, tiled=True)
    mine = step.reshape(tile_count, pixels)
    own = unit_rows(raw)
    place = lax.axis_index("atom")
    core = place % 2
    chips = atom_count // 2
    chip = place // 2
    other = lax.ppermute(mine, "atom", [(i, i ^ 1) for i in range(atom_count)])
    pair = jnp.concatenate([mine, other])
    pieces = [pair]
    for hop in range(1, chips):
        pieces.append(lax.ppermute(pair, "atom", [(i, ((i // 2 + hop) % chips) * 2 + i % 2) for i in range(atom_count)]))
    every = jnp.concatenate(pieces, axis=0).reshape(atom_count, tile_count * pixels)

    image_spec = forward(images.reshape(1, tiles_here, pixels), table).reshape(tiles_here, width)
    slot_count = tiles_here * ACT
    flat_ids = active.reshape(slot_count)
    where_held = ((chip - flat_ids // 2) % chips) * 2 + (flat_ids % 2 != core).astype(jnp.int32)
    chosen_atoms = unit_rows(jnp.take(every, where_held, axis=0).reshape(slot_count * BLK, pixels))
    rows = ACT * BLK
    chosen = forward(chosen_atoms, table).reshape(tiles_here, rows, width)
    chosen_real, chosen_imag = parts(chosen)
    power = jnp.sum(chosen_real * chosen_real + chosen_imag * chosen_imag, axis=1)
    bound = jnp.max(power, axis=1) + epsilon
    rate = (1.0 / bound)[:, None, None]
    limit = rate * (shrink_scale * SIDE)
    weights = momentum_weights(ITERS)

    prior = None
    guess = None
    guess_spec = None
    for sweep in range(ITERS):
        if guess is None:
            residual_spec = -image_spec
        else:
            residual_spec = product_sum(chosen, guess_spec) - image_spec
        gradient = inverse(conj_times(chosen, residual_spec[:, None, :]).reshape(tiles_here * rows, width), table, weight)
        gradient = gradient.reshape(tiles_here, rows, pixels)
        if guess is None:
            moved = -(rate * gradient)
        else:
            moved = guess - rate * gradient
        fresh = moved - jnp.clip(moved, -limit, limit)
        if prior is None:
            guess = fresh + weights[sweep] * fresh
        else:
            guess = fresh + weights[sweep] * (fresh - prior)
        prior = fresh
        if sweep + 1 < ITERS:
            guess_spec = forward(guess.reshape(tiles_here * rows, pixels), table).reshape(tiles_here, rows, width)

    code_spec = forward(prior.reshape(tiles_here * rows, pixels), table).reshape(tiles_here, rows, width)
    recon_spec = product_sum(chosen, code_spec)
    residual_spec = recon_spec - image_spec
    slot_terms = conj_times(code_spec, residual_spec[:, None, :]).reshape(slot_count, BLK * width)
    member = (jnp.arange(NBLK, dtype=jnp.int32)[:, None] == flat_ids[None, :]).astype(jnp.float32)
    block_spec = jnp.dot(member, slot_terms, precision=highest, preferred_element_type=jnp.float32)
    both = inverse(jnp.concatenate([block_spec.reshape(NBLK * BLK, width), recon_spec], axis=0), table, weight)
    partial = both[:NBLK * BLK].reshape(NBLK, BLK, pixels)
    recon = both[NBLK * BLK:]

    paired = partial.reshape(chips, 2, BLK, pixels)
    keep = lax.dynamic_index_in_dim(paired, core, axis=1, keepdims=False)
    give = lax.dynamic_index_in_dim(paired, 1 - core, axis=1, keepdims=False)
    summed = keep + lax.ppermute(give, "atom", [(i, i ^ 1) for i in range(atom_count)])
    arrived = lax.dynamic_index_in_dim(summed, chip, axis=0, keepdims=False)
    for hop in range(1, chips):
        sent = lax.dynamic_index_in_dim(summed, (chip + hop) % chips, axis=0, keepdims=False)
        arrived = arrived + lax.ppermute(sent, "atom", [(i, ((i // 2 + hop) % chips) * 2 + i % 2) for i in range(atom_count)])
    arrived = arrived.reshape(tile_count, 1, pixels)
    atom_grad = jnp.sum(lax.all_to_all(arrived, "tile", 0, 0, tiled=True), axis=0)

    scale = jnp.sqrt(jnp.mean(atom_grad * atom_grad, axis=-1, keepdims=True) + epsilon)
    atoms = unit_rows(own - step_ratio * atom_grad / scale)
    return (recon, atoms.reshape(dictionary.shape))


def solution(mesh):
    in_specs = (P(("tile", "atom"), None), P(("tile", "atom"), None), P("atom", "tile", None))
    out_specs = (P(("tile", "atom"), None), P("atom", "tile", None))
    return jax.shard_map(
        on_device, mesh=mesh, in_specs=in_specs, out_specs=out_specs, check_vma=False
    )
```

```python
import math

import numpy as np
import jax
import jax.numpy as jnp
from jax import lax
from jax.sharding import PartitionSpec as P

SIDE = 32
BLK = 32
NBLK = 8
ACT = 2
ITERS = 2

shrink_scale = 0.5
step_ratio = 0.5
epsilon = 1e-06
highest = lax.Precision.HIGHEST
fast = lax.Precision.HIGH

HALF = SIDE // 2 + 1
USED = SIDE * HALF
PART = 640


def momentum_weights(count):
    weights = []
    current = 1.0
    for sweep in range(count):
        following = (1.0 + math.sqrt(1.0 + 4.0 * current * current)) / 2.0
        weights.append((current - 1.0) / following)
        current = following
    return weights


def unit_rows(values):
    return values / jnp.sqrt(jnp.mean(values * values, axis=-1, keepdims=True) + epsilon)


def half_table():
    side = np.arange(SIDE)
    phase = (side[:, None, None, None] * side[None, None, :, None]
             + side[None, :, None, None] * np.arange(HALF)[None, None, None, :]) % SIDE
    angle = phase * (2.0 * np.pi / SIDE)
    table = np.zeros((SIDE * SIDE, 2 * PART), np.float32)
    table[:, :USED] = np.cos(angle).reshape(SIDE * SIDE, USED)
    table[:, PART:PART + USED] = -np.sin(angle).reshape(SIDE * SIDE, USED)
    column = np.arange(HALF)
    pair = np.where((column == 0) | (column == SIDE // 2), 1.0, 2.0) / (SIDE * SIDE)
    weight = np.zeros((2 * PART,), np.float32)
    weight[:USED] = np.tile(pair, SIDE)
    weight[PART:PART + USED] = np.tile(pair, SIDE)
    return table, weight


def forward(values, table):
    return jnp.dot(values, table, precision=fast, preferred_element_type=jnp.float32)


def inverse(spectra, table, weight):
    return lax.dot_general(
        spectra * weight, table, (((spectra.ndim - 1,), (1,)), ((), ())),
        precision=fast, preferred_element_type=jnp.float32,
    )


def parts(packed):
    return (packed[..., :PART], packed[..., PART:])


def conj_times(first, second):
    first_real, first_imag = parts(first)
    second_real, second_imag = parts(second)
    real_part = first_real * second_real + first_imag * second_imag
    imag_part = first_real * second_imag - first_imag * second_real
    return jnp.concatenate([real_part, imag_part], axis=-1)


def product_sum(atom_spec, code_spec):
    atom_real, atom_imag = parts(atom_spec)
    code_real, code_imag = parts(code_spec)
    real_sum = jnp.sum(atom_real * code_real - atom_imag * code_imag, axis=1)
    imag_sum = jnp.sum(atom_real * code_imag + atom_imag * code_real, axis=1)
    return jnp.concatenate([real_sum, imag_sum], axis=-1)


def on_device(images, active, dictionary):
    tiles_here, pixels = images.shape
    tile_count = lax.axis_size("tile")
    atom_count = lax.axis_size("atom")
    table_host, weight_host = half_table()
    table = jnp.asarray(table_host)
    weight = jnp.asarray(weight_host)
    table, weight = lax.optimization_barrier((table, weight))
    width = table.shape[1]

    raw = dictionary.reshape(1, pixels)
    step = lax.all_to_all(jnp.broadcast_to(raw[None], (tile_count, 1, pixels)), "tile", 0, 0, tiled=True)
    mine = step.reshape(tile_count, pixels)
    own = unit_rows(raw)
    place = lax.axis_index("atom")
    core = place % 2
    chips = atom_count // 2
    chip = place // 2
    other = lax.ppermute(mine, "atom", [(i, i ^ 1) for i in range(atom_count)])
    pair = jnp.concatenate([mine, other])
    pieces = [pair]
    for hop in range(1, chips):
        pieces.append(lax.ppermute(pair, "atom", [(i, ((i // 2 + hop) % chips) * 2 + i % 2) for i in range(atom_count)]))
    every = jnp.concatenate(pieces, axis=0).reshape(atom_count, tile_count, pixels)

    image_spec = forward(images.reshape(1, tiles_here, pixels), table).reshape(tiles_here, width)
    slot_count = tiles_here * ACT
    flat_ids = active.reshape(slot_count)
    where_held = ((chip - flat_ids // 2) % chips) * 2 + (flat_ids % 2 != core).astype(jnp.int32)
    chosen_atoms = unit_rows(jnp.take(every, where_held, axis=0).reshape(slot_count * BLK, pixels))
    rows = ACT * BLK
    chosen = forward(chosen_atoms, table).reshape(tiles_here, rows, width)
    chosen_real, chosen_imag = parts(chosen)
    power = jnp.sum(chosen_real * chosen_real + chosen_imag * chosen_imag, axis=1)
    bound = jnp.max(power, axis=1) + epsilon
    rate = (1.0 / bound)[:, None, None]
    limit = rate * (shrink_scale * SIDE)
    weights = momentum_weights(ITERS)

    prior = None
    guess = None
    guess_spec = None
    for sweep in range(ITERS):
        if guess is None:
            residual_spec = -image_spec
        else:
            residual_spec = product_sum(chosen, guess_spec) - image_spec
        gradient = inverse(conj_times(chosen, residual_spec[:, None, :]).reshape(tiles_here * rows, width), table, weight)
        gradient = gradient.reshape(tiles_here, rows, pixels)
        if guess is None:
            moved = -(rate * gradient)
        else:
            moved = guess - rate * gradient
        fresh = moved - jnp.clip(moved, -limit, limit)
        if prior is None:
            guess = fresh + weights[sweep] * fresh
        else:
            guess = fresh + weights[sweep] * (fresh - prior)
        prior = fresh
        if sweep + 1 < ITERS:
            guess_spec = forward(guess.reshape(tiles_here * rows, pixels), table).reshape(tiles_here, rows, width)

    code_spec = forward(prior.reshape(tiles_here * rows, pixels), table).reshape(tiles_here, rows, width)
    recon_spec = product_sum(chosen, code_spec)
    residual_spec = recon_spec - image_spec
    slot_terms = conj_times(code_spec, residual_spec[:, None, :]).reshape(slot_count, BLK, width)
    member = (jnp.arange(NBLK, dtype=jnp.int32)[:, None] == flat_ids[None, :]).astype(jnp.float32)
    block_spec = jnp.einsum("bs,skx->bkx", member, slot_terms, precision=highest, preferred_element_type=jnp.float32)
    both = inverse(jnp.concatenate([block_spec.reshape(NBLK * BLK, width), recon_spec], axis=0), table, weight)
    partial = both[:NBLK * BLK].reshape(NBLK, BLK, pixels)
    recon = both[NBLK * BLK:]

    paired = partial.reshape(chips, 2, BLK, pixels)
    keep = lax.dynamic_index_in_dim(paired, core, axis=1, keepdims=False)
    give = lax.dynamic_index_in_dim(paired, 1 - core, axis=1, keepdims=False)
    summed = keep + lax.ppermute(give, "atom", [(i, i ^ 1) for i in range(atom_count)])
    arrived = lax.dynamic_index_in_dim(summed, chip, axis=0, keepdims=False)
    for hop in range(1, chips):
        sent = lax.dynamic_index_in_dim(summed, (chip + hop) % chips, axis=0, keepdims=False)
        arrived = arrived + lax.ppermute(sent, "atom", [(i, ((i // 2 + hop) % chips) * 2 + i % 2) for i in range(atom_count)])
    arrived = arrived.reshape(tile_count, 1, pixels)
    atom_grad = jnp.sum(lax.all_to_all(arrived, "tile", 0, 0, tiled=True), axis=0)

    scale = jnp.sqrt(jnp.mean(atom_grad * atom_grad, axis=-1, keepdims=True) + epsilon)
    atoms = unit_rows(own - step_ratio * atom_grad / scale)
    return (recon, atoms.reshape(dictionary.shape))


def solution(mesh):
    in_specs = (P(("tile", "atom"), None), P(("tile", "atom"), None), P("atom", "tile", None))
    out_specs = (P(("tile", "atom"), None), P("atom", "tile", None))
    return jax.shard_map(
        on_device, mesh=mesh, in_specs=in_specs, out_specs=out_specs, check_vma=False
    )
```

```python
import math

import numpy as np
import jax
import jax.numpy as jnp
from jax import lax
from jax.sharding import PartitionSpec as P

SIDE = 32
BLK = 32
NBLK = 8
ACT = 2
ITERS = 2

shrink_scale = 0.5
step_ratio = 0.5
epsilon = 1e-06
highest = lax.Precision.HIGHEST
fast = lax.Precision.HIGH

HALF = SIDE // 2 + 1
USED = SIDE * HALF
PART = 640


def momentum_weights(count):
    weights = []
    current = 1.0
    for sweep in range(count):
        following = (1.0 + math.sqrt(1.0 + 4.0 * current * current)) / 2.0
        weights.append((current - 1.0) / following)
        current = following
    return weights


def unit_rows(values):
    return values / jnp.sqrt(jnp.mean(values * values, axis=-1, keepdims=True) + epsilon)


def half_table():
    side = np.arange(SIDE)
    phase = (side[:, None, None, None] * side[None, None, :, None]
             + side[None, :, None, None] * np.arange(HALF)[None, None, None, :]) % SIDE
    angle = phase * (2.0 * np.pi / SIDE)
    table = np.zeros((SIDE * SIDE, 2 * PART), np.float32)
    table[:, :USED] = np.cos(angle).reshape(SIDE * SIDE, USED)
    table[:, PART:PART + USED] = -np.sin(angle).reshape(SIDE * SIDE, USED)
    column = np.arange(HALF)
    pair = np.where((column == 0) | (column == SIDE // 2), 1.0, 2.0) / (SIDE * SIDE)
    weight = np.zeros((2 * PART,), np.float32)
    weight[:USED] = np.tile(pair, SIDE)
    weight[PART:PART + USED] = np.tile(pair, SIDE)
    return table, weight


def forward(values, table):
    return jnp.dot(values, table, precision=fast, preferred_element_type=jnp.float32)


def inverse(spectra, table, weight):
    return lax.dot_general(
        spectra * weight, table, (((spectra.ndim - 1,), (1,)), ((), ())),
        precision=fast, preferred_element_type=jnp.float32,
    )


def parts(packed):
    return (packed[..., :PART], packed[..., PART:])


def conj_times(first, second):
    first_real, first_imag = parts(first)
    second_real, second_imag = parts(second)
    real_part = first_real * second_real + first_imag * second_imag
    imag_part = first_real * second_imag - first_imag * second_real
    return jnp.concatenate([real_part, imag_part], axis=-1)


def product_sum(atom_spec, code_spec):
    atom_real, atom_imag = parts(atom_spec)
    code_real, code_imag = parts(code_spec)
    real_sum = jnp.sum(atom_real * code_real - atom_imag * code_imag, axis=1)
    imag_sum = jnp.sum(atom_real * code_imag + atom_imag * code_real, axis=1)
    return jnp.concatenate([real_sum, imag_sum], axis=-1)


def on_device(images, active, dictionary):
    tiles_here, pixels = images.shape
    tile_count = lax.axis_size("tile")
    atom_count = lax.axis_size("atom")
    table_host, weight_host = half_table()
    table = jnp.asarray(table_host)
    weight = jnp.asarray(weight_host)
    table, weight = lax.optimization_barrier((table, weight))
    width = table.shape[1]

    raw = dictionary.reshape(1, pixels)
    dense = raw.reshape(1, 8, pixels // 8)
    step = lax.all_to_all(jnp.broadcast_to(dense, (tile_count, 8, pixels // 8)), "tile", 0, 0, tiled=True)
    mine = step.reshape(tile_count, pixels)
    own = unit_rows(raw)
    place = lax.axis_index("atom")
    core = place % 2
    chips = atom_count // 2
    chip = place // 2
    other = lax.ppermute(mine, "atom", [(i, i ^ 1) for i in range(atom_count)])
    pair = jnp.concatenate([mine, other])
    pieces = [pair]
    for hop in range(1, chips):
        pieces.append(lax.ppermute(pair, "atom", [(i, ((i // 2 + hop) % chips) * 2 + i % 2) for i in range(atom_count)]))
    every = jnp.concatenate(pieces, axis=0).reshape(atom_count, tile_count, pixels)

    image_spec = forward(images.reshape(1, tiles_here, pixels), table).reshape(tiles_here, width)
    slot_count = tiles_here * ACT
    flat_ids = active.reshape(slot_count)
    where_held = ((chip - flat_ids // 2) % chips) * 2 + (flat_ids % 2 != core).astype(jnp.int32)
    chosen_atoms = unit_rows(jnp.take(every, where_held, axis=0).reshape(slot_count * BLK, pixels))
    rows = ACT * BLK
    chosen = forward(chosen_atoms, table).reshape(tiles_here, rows, width)
    chosen_real, chosen_imag = parts(chosen)
    power = jnp.sum(chosen_real * chosen_real + chosen_imag * chosen_imag, axis=1)
    bound = jnp.max(power, axis=1) + epsilon
    rate = (1.0 / bound)[:, None, None]
    limit = rate * (shrink_scale * SIDE)
    weights = momentum_weights(ITERS)

    prior = None
    guess = None
    guess_spec = None
    for sweep in range(ITERS):
        if guess is None:
            residual_spec = -image_spec
        else:
            residual_spec = product_sum(chosen, guess_spec) - image_spec
        gradient = inverse(conj_times(chosen, residual_spec[:, None, :]).reshape(tiles_here * rows, width), table, weight)
        gradient = gradient.reshape(tiles_here, rows, pixels)
        if guess is None:
            moved = -(rate * gradient)
        else:
            moved = guess - rate * gradient
        fresh = moved - jnp.clip(moved, -limit, limit)
        if prior is None:
            guess = fresh + weights[sweep] * fresh
        else:
            guess = fresh + weights[sweep] * (fresh - prior)
        prior = fresh
        if sweep + 1 < ITERS:
            guess_spec = forward(guess.reshape(tiles_here * rows, pixels), table).reshape(tiles_here, rows, width)

    code_spec = forward(prior.reshape(tiles_here * rows, pixels), table).reshape(tiles_here, rows, width)
    recon_spec = product_sum(chosen, code_spec)
    residual_spec = recon_spec - image_spec
    slot_terms = conj_times(code_spec, residual_spec[:, None, :]).reshape(slot_count, BLK, width)
    member = (jnp.arange(NBLK, dtype=jnp.int32)[:, None] == flat_ids[None, :]).astype(jnp.float32)
    block_spec = jnp.einsum("bs,skx->bkx", member, slot_terms, precision=highest, preferred_element_type=jnp.float32)
    both = inverse(jnp.concatenate([block_spec.reshape(NBLK * BLK, width), recon_spec], axis=0), table, weight)
    partial = both[:NBLK * BLK].reshape(NBLK, BLK, pixels)
    recon = both[NBLK * BLK:]

    paired = partial.reshape(chips, 2, BLK, pixels)
    keep = lax.dynamic_index_in_dim(paired, core, axis=1, keepdims=False)
    give = lax.dynamic_index_in_dim(paired, 1 - core, axis=1, keepdims=False)
    summed = keep + lax.ppermute(give, "atom", [(i, i ^ 1) for i in range(atom_count)])
    arrived = lax.dynamic_index_in_dim(summed, chip, axis=0, keepdims=False)
    for hop in range(1, chips):
        sent = lax.dynamic_index_in_dim(summed, (chip + hop) % chips, axis=0, keepdims=False)
        arrived = arrived + lax.ppermute(sent, "atom", [(i, ((i // 2 + hop) % chips) * 2 + i % 2) for i in range(atom_count)])
    arrived = arrived.reshape(tile_count, 1, pixels)
    atom_grad = jnp.sum(lax.all_to_all(arrived, "tile", 0, 0, tiled=True), axis=0)

    scale = jnp.sqrt(jnp.mean(atom_grad * atom_grad, axis=-1, keepdims=True) + epsilon)
    atoms = unit_rows(own - step_ratio * atom_grad / scale)
    return (recon, atoms.reshape(dictionary.shape))


def solution(mesh):
    in_specs = (P(("tile", "atom"), None), P(("tile", "atom"), None), P("atom", "tile", None))
    out_specs = (P(("tile", "atom"), None), P("atom", "tile", None))
    return jax.shard_map(
        on_device, mesh=mesh, in_specs=in_specs, out_specs=out_specs, check_vma=False
    )
```

```python
import math

import numpy as np
import jax
import jax.numpy as jnp
from jax import lax
from jax.sharding import PartitionSpec as P

SIDE = 32
BLK = 32
NBLK = 8
ACT = 2
ITERS = 2

shrink_scale = 0.5
step_ratio = 0.5
epsilon = 1e-06
highest = lax.Precision.HIGHEST
fast = lax.Precision.HIGH

HALF = SIDE // 2 + 1
USED = SIDE * HALF
PART = 640


def momentum_weights(count):
    weights = []
    current = 1.0
    for sweep in range(count):
        following = (1.0 + math.sqrt(1.0 + 4.0 * current * current)) / 2.0
        weights.append((current - 1.0) / following)
        current = following
    return weights


def unit_rows(values):
    return values / jnp.sqrt(jnp.mean(values * values, axis=-1, keepdims=True) + epsilon)


def half_table():
    side = np.arange(SIDE)
    phase = (side[:, None, None, None] * side[None, None, :, None]
             + side[None, :, None, None] * np.arange(HALF)[None, None, None, :]) % SIDE
    angle = phase * (2.0 * np.pi / SIDE)
    table = np.zeros((SIDE * SIDE, 2 * PART), np.float32)
    table[:, :USED] = np.cos(angle).reshape(SIDE * SIDE, USED)
    table[:, PART:PART + USED] = -np.sin(angle).reshape(SIDE * SIDE, USED)
    column = np.arange(HALF)
    pair = np.where((column == 0) | (column == SIDE // 2), 1.0, 2.0) / (SIDE * SIDE)
    weight = np.zeros((2 * PART,), np.float32)
    weight[:USED] = np.tile(pair, SIDE)
    weight[PART:PART + USED] = np.tile(pair, SIDE)
    return table, weight


def forward(values, table):
    return jnp.dot(values, table, precision=fast, preferred_element_type=jnp.float32)


def inverse(spectra, table, weight):
    return lax.dot_general(
        spectra * weight, table, (((spectra.ndim - 1,), (1,)), ((), ())),
        precision=fast, preferred_element_type=jnp.float32,
    )


def parts(packed):
    return (packed[..., :PART], packed[..., PART:])


def conj_times(first, second):
    first_real, first_imag = parts(first)
    second_real, second_imag = parts(second)
    real_part = first_real * second_real + first_imag * second_imag
    imag_part = first_real * second_imag - first_imag * second_real
    return jnp.concatenate([real_part, imag_part], axis=-1)


def product_sum(atom_spec, code_spec):
    atom_real, atom_imag = parts(atom_spec)
    code_real, code_imag = parts(code_spec)
    real_sum = jnp.sum(atom_real * code_real - atom_imag * code_imag, axis=1)
    imag_sum = jnp.sum(atom_real * code_imag + atom_imag * code_real, axis=1)
    return jnp.concatenate([real_sum, imag_sum], axis=-1)


def on_device(images, active, dictionary):
    tiles_here, pixels = images.shape
    tile_count = lax.axis_size("tile")
    atom_count = lax.axis_size("atom")
    table_host, weight_host = half_table()
    table = jnp.asarray(table_host)
    weight = jnp.asarray(weight_host)
    table, weight = lax.optimization_barrier((table, weight))
    width = table.shape[1]

    raw = dictionary.reshape(1, pixels)
    dense = raw.reshape(1, 8, pixels // 8)
    step = lax.all_to_all(jnp.broadcast_to(dense, (tile_count, 8, pixels // 8)), "tile", 0, 0, tiled=True)
    mine = step.reshape(tile_count, pixels)
    own = unit_rows(raw)
    place = lax.axis_index("atom")
    core = place % 2
    chips = atom_count // 2
    chip = place // 2
    other = lax.ppermute(mine, "atom", [(i, i ^ 1) for i in range(atom_count)])
    pair = jnp.concatenate([mine, other])
    pieces = [pair]
    for hop in range(1, chips):
        pieces.append(lax.ppermute(pair, "atom", [(i, ((i // 2 + hop) % chips) * 2 + i % 2) for i in range(atom_count)]))
    every = jnp.concatenate(pieces, axis=0).reshape(atom_count, tile_count, pixels)

    image_spec = forward(images.reshape(1, tiles_here, pixels), table).reshape(tiles_here, width)
    slot_count = tiles_here * ACT
    flat_ids = active.reshape(slot_count)
    where_held = ((chip - flat_ids // 2) % chips) * 2 + (flat_ids % 2 != core).astype(jnp.int32)
    chosen_atoms = unit_rows(jnp.take(every, where_held, axis=0).reshape(slot_count * BLK, pixels))
    rows = ACT * BLK
    chosen = forward(chosen_atoms, table).reshape(tiles_here, rows, width)
    chosen_real, chosen_imag = parts(chosen)
    power = jnp.sum(chosen_real * chosen_real + chosen_imag * chosen_imag, axis=1)
    bound = jnp.max(power, axis=1) + epsilon
    rate = (1.0 / bound)[:, None, None]
    limit = rate * (shrink_scale * SIDE)
    weights = momentum_weights(ITERS)

    prior = None
    guess = None
    guess_spec = None
    for sweep in range(ITERS):
        if guess is None:
            residual_spec = -image_spec
        else:
            residual_spec = product_sum(chosen, guess_spec) - image_spec
        gradient = inverse(conj_times(chosen, residual_spec[:, None, :]).reshape(tiles_here * rows, width), table, weight)
        gradient = gradient.reshape(tiles_here, rows, pixels)
        if guess is None:
            moved = -(rate * gradient)
        else:
            moved = guess - rate * gradient
        fresh = moved - jnp.clip(moved, -limit, limit)
        if prior is None:
            guess = fresh + weights[sweep] * fresh
        else:
            guess = fresh + weights[sweep] * (fresh - prior)
        prior = fresh
        if sweep + 1 < ITERS:
            guess_spec = forward(guess.reshape(tiles_here * rows, pixels), table).reshape(tiles_here, rows, width)

    code_spec = forward(prior.reshape(tiles_here * rows, pixels), table).reshape(tiles_here, rows, width)
    recon_spec = product_sum(chosen, code_spec)
    residual_spec = recon_spec - image_spec
    slot_terms = conj_times(code_spec, residual_spec[:, None, :]).reshape(slot_count, BLK, width)
    member = (jnp.arange(NBLK, dtype=jnp.int32)[:, None] == flat_ids[None, :]).astype(jnp.float32)
    block_spec = jnp.einsum("bs,skx->bkx", member, slot_terms, precision=highest, preferred_element_type=jnp.float32)
    both = inverse(jnp.concatenate([block_spec.reshape(NBLK * BLK, width), recon_spec], axis=0), table, weight)
    partial = both[:NBLK * BLK].reshape(NBLK, BLK, pixels)
    recon = both[NBLK * BLK:]

    paired = partial.reshape(chips, 2, BLK, pixels)
    keep = lax.dynamic_index_in_dim(paired, core, axis=1, keepdims=False)
    give = lax.dynamic_index_in_dim(paired, 1 - core, axis=1, keepdims=False)
    summed = keep + lax.ppermute(give, "atom", [(i, i ^ 1) for i in range(atom_count)])
    arrived = lax.dynamic_index_in_dim(summed, chip, axis=0, keepdims=False)
    for hop in range(1, chips):
        sent = lax.dynamic_index_in_dim(summed, (chip + hop) % chips, axis=0, keepdims=False)
        arrived = arrived + lax.ppermute(sent, "atom", [(i, ((i // 2 + hop) % chips) * 2 + i % 2) for i in range(atom_count)])
    arrived = arrived.reshape(tile_count, 1, pixels)
    atom_grad = jnp.sum(lax.all_to_all(arrived, "tile", 0, 0, tiled=True), axis=0)

    grad_square = jnp.mean(atom_grad * atom_grad, axis=-1, keepdims=True)
    cross = jnp.mean(own * atom_grad, axis=-1, keepdims=True)
    own_square = jnp.mean(own * own, axis=-1, keepdims=True)
    scale = jnp.sqrt(grad_square + epsilon)
    shift = step_ratio / scale
    moved_square = own_square - 2.0 * shift * cross + shift * shift * grad_square
    atoms = (own - shift * atom_grad) / jnp.sqrt(moved_square + epsilon)
    return (recon, atoms.reshape(dictionary.shape))


def solution(mesh):
    in_specs = (P(("tile", "atom"), None), P(("tile", "atom"), None), P("atom", "tile", None))
    out_specs = (P(("tile", "atom"), None), P("atom", "tile", None))
    return jax.shard_map(
        on_device, mesh=mesh, in_specs=in_specs, out_specs=out_specs, check_vma=False
    )
```

```python
import math

import numpy as np
import jax
import jax.numpy as jnp
from jax import lax
from jax.sharding import PartitionSpec as P

SIDE = 32
BLK = 32
NBLK = 8
ACT = 2
ITERS = 2

shrink_scale = 0.5
step_ratio = 0.5
epsilon = 1e-06
highest = lax.Precision.HIGHEST
fast = lax.Precision.HIGH

HALF = SIDE // 2 + 1
USED = SIDE * HALF
PART = 640


def momentum_weights(count):
    weights = []
    current = 1.0
    for sweep in range(count):
        following = (1.0 + math.sqrt(1.0 + 4.0 * current * current)) / 2.0
        weights.append((current - 1.0) / following)
        current = following
    return weights


def unit_rows(values):
    return values / jnp.sqrt(jnp.mean(values * values, axis=-1, keepdims=True) + epsilon)


def half_table():
    side = np.arange(SIDE)
    phase = (side[:, None, None, None] * side[None, None, :, None]
             + side[None, :, None, None] * np.arange(HALF)[None, None, None, :]) % SIDE
    angle = phase * (2.0 * np.pi / SIDE)
    table = np.zeros((SIDE * SIDE, 2 * PART), np.float32)
    table[:, :USED] = np.cos(angle).reshape(SIDE * SIDE, USED)
    table[:, PART:PART + USED] = -np.sin(angle).reshape(SIDE * SIDE, USED)
    column = np.arange(HALF)
    pair = np.where((column == 0) | (column == SIDE // 2), 1.0, 2.0) / (SIDE * SIDE)
    weight = np.zeros((2 * PART,), np.float32)
    weight[:USED] = np.tile(pair, SIDE)
    weight[PART:PART + USED] = np.tile(pair, SIDE)
    return table, weight


def forward(values, table):
    return jnp.dot(values, table, precision=fast, preferred_element_type=jnp.float32)


def inverse(spectra, table, weight):
    return lax.dot_general(
        spectra * weight, table, (((spectra.ndim - 1,), (1,)), ((), ())),
        precision=fast, preferred_element_type=jnp.float32,
    )


def parts(packed):
    return (packed[..., :PART], packed[..., PART:])


def conj_times(first, second):
    first_real, first_imag = parts(first)
    second_real, second_imag = parts(second)
    real_part = first_real * second_real + first_imag * second_imag
    imag_part = first_real * second_imag - first_imag * second_real
    return jnp.concatenate([real_part, imag_part], axis=-1)


def product_sum(atom_spec, code_spec):
    atom_real, atom_imag = parts(atom_spec)
    code_real, code_imag = parts(code_spec)
    real_sum = jnp.sum(atom_real * code_real - atom_imag * code_imag, axis=1)
    imag_sum = jnp.sum(atom_real * code_imag + atom_imag * code_real, axis=1)
    return jnp.concatenate([real_sum, imag_sum], axis=-1)


def on_device(images, active, dictionary):
    tiles_here, pixels = images.shape
    tile_count = lax.axis_size("tile")
    atom_count = lax.axis_size("atom")
    table_host, weight_host = half_table()
    table = jnp.asarray(table_host)
    weight = jnp.asarray(weight_host)
    table, weight = lax.optimization_barrier((table, weight))
    width = table.shape[1]

    raw = dictionary.reshape(1, pixels)
    dense = raw.reshape(1, 8, pixels // 8)
    step = lax.all_to_all(jnp.broadcast_to(dense, (tile_count, 8, pixels // 8)), "tile", 0, 0, tiled=True)
    mine = step.reshape(tile_count, pixels)
    own = unit_rows(raw)
    place = lax.axis_index("atom")
    core = place % 2
    chips = atom_count // 2
    chip = place // 2
    other = lax.ppermute(mine, "atom", [(i, i ^ 1) for i in range(atom_count)])
    pair = jnp.concatenate([mine, other])
    pieces = [pair]
    for hop in range(1, chips):
        pieces.append(lax.ppermute(pair, "atom", [(i, ((i // 2 + hop) % chips) * 2 + i % 2) for i in range(atom_count)]))
    every = jnp.concatenate(pieces, axis=0).reshape(atom_count, tile_count, pixels)

    image_spec = forward(images.reshape(1, tiles_here, pixels), table).reshape(tiles_here, width)
    slot_count = tiles_here * ACT
    flat_ids = active.reshape(slot_count)
    where_held = ((chip - flat_ids // 2) % chips) * 2 + (flat_ids % 2 != core).astype(jnp.int32)
    chosen_atoms = unit_rows(jnp.take(every, where_held, axis=0).reshape(slot_count * BLK, pixels))
    rows = ACT * BLK
    chosen = forward(chosen_atoms, table).reshape(tiles_here, rows, width)
    chosen_real, chosen_imag = parts(chosen)
    power = jnp.sum(chosen_real * chosen_real + chosen_imag * chosen_imag, axis=1)
    bound = jnp.max(power, axis=1) + epsilon
    rate = (1.0 / bound)[:, None, None]
    limit = rate * (shrink_scale * SIDE)
    weights = momentum_weights(ITERS)

    prior = None
    guess = None
    guess_spec = None
    for sweep in range(ITERS):
        if guess is None:
            residual_spec = -image_spec
        else:
            residual_spec = product_sum(chosen, guess_spec) - image_spec
        gradient = inverse(conj_times(chosen, residual_spec[:, None, :]).reshape(tiles_here * rows, width), table, weight)
        gradient = gradient.reshape(tiles_here, rows, pixels)
        if guess is None:
            moved = -(rate * gradient)
        else:
            moved = guess - rate * gradient
        fresh = moved - jnp.clip(moved, -limit, limit)
        if prior is None:
            guess = fresh + weights[sweep] * fresh
        else:
            guess = fresh + weights[sweep] * (fresh - prior)
        prior = fresh
        if sweep + 1 < ITERS:
            guess_spec = forward(guess.reshape(tiles_here * rows, pixels), table).reshape(tiles_here, rows, width)

    code_spec = forward(prior.reshape(tiles_here * rows, pixels), table).reshape(tiles_here, rows, width)
    recon_spec = product_sum(chosen, code_spec)
    residual_spec = recon_spec - image_spec
    slot_terms = conj_times(code_spec, residual_spec[:, None, :]).reshape(slot_count, BLK, width)
    member = (jnp.arange(NBLK, dtype=jnp.int32)[:, None] == flat_ids[None, :]).astype(jnp.float32)
    block_spec = jnp.einsum("bs,skx->bkx", member, slot_terms, precision=fast, preferred_element_type=jnp.float32)
    both = inverse(jnp.concatenate([block_spec.reshape(NBLK * BLK, width), recon_spec], axis=0), table, weight)
    partial = both[:NBLK * BLK].reshape(NBLK, BLK, pixels)
    recon = both[NBLK * BLK:]

    paired = partial.reshape(chips, 2, BLK, pixels)
    keep = lax.dynamic_index_in_dim(paired, core, axis=1, keepdims=False)
    give = lax.dynamic_index_in_dim(paired, 1 - core, axis=1, keepdims=False)
    summed = keep + lax.ppermute(give, "atom", [(i, i ^ 1) for i in range(atom_count)])
    arrived = lax.dynamic_index_in_dim(summed, chip, axis=0, keepdims=False)
    for hop in range(1, chips):
        sent = lax.dynamic_index_in_dim(summed, (chip + hop) % chips, axis=0, keepdims=False)
        arrived = arrived + lax.ppermute(sent, "atom", [(i, ((i // 2 + hop) % chips) * 2 + i % 2) for i in range(atom_count)])
    arrived = arrived.reshape(tile_count, 1, pixels)
    atom_grad = jnp.sum(lax.all_to_all(arrived, "tile", 0, 0, tiled=True), axis=0)

    scale = jnp.sqrt(jnp.mean(atom_grad * atom_grad, axis=-1, keepdims=True) + epsilon)
    atoms = unit_rows(own - step_ratio * atom_grad / scale)
    return (recon, atoms.reshape(dictionary.shape))


def solution(mesh):
    in_specs = (P(("tile", "atom"), None), P(("tile", "atom"), None), P("atom", "tile", None))
    out_specs = (P(("tile", "atom"), None), P("atom", "tile", None))
    return jax.shard_map(
        on_device, mesh=mesh, in_specs=in_specs, out_specs=out_specs, check_vma=False
    )
```

```python
import math

import numpy as np
import jax
import jax.numpy as jnp
from jax import lax
from jax.sharding import PartitionSpec as P

SIDE = 32
BLK = 32
NBLK = 8
ACT = 2
ITERS = 2

shrink_scale = 0.5
step_ratio = 0.5
epsilon = 1e-06
highest = lax.Precision.HIGHEST
fast = lax.Precision.HIGH

HALF = SIDE // 2 + 1
USED = SIDE * HALF
PART = 640


def momentum_weights(count):
    weights = []
    current = 1.0
    for sweep in range(count):
        following = (1.0 + math.sqrt(1.0 + 4.0 * current * current)) / 2.0
        weights.append((current - 1.0) / following)
        current = following
    return weights


def unit_rows(values):
    return values / jnp.sqrt(jnp.mean(values * values, axis=-1, keepdims=True) + epsilon)


def half_table():
    side = np.arange(SIDE)
    phase = (side[:, None, None, None] * side[None, None, :, None]
             + side[None, :, None, None] * np.arange(HALF)[None, None, None, :]) % SIDE
    angle = phase * (2.0 * np.pi / SIDE)
    table = np.zeros((SIDE * SIDE, 2 * PART), np.float32)
    table[:, :USED] = np.cos(angle).reshape(SIDE * SIDE, USED)
    table[:, PART:PART + USED] = -np.sin(angle).reshape(SIDE * SIDE, USED)
    column = np.arange(HALF)
    pair = np.where((column == 0) | (column == SIDE // 2), 1.0, 2.0) / (SIDE * SIDE)
    weight = np.zeros((2 * PART,), np.float32)
    weight[:USED] = np.tile(pair, SIDE)
    weight[PART:PART + USED] = np.tile(pair, SIDE)
    return table, weight


def forward(values, table):
    return jnp.dot(values, table, precision=fast, preferred_element_type=jnp.float32)


def inverse(spectra, table, weight):
    return lax.dot_general(
        spectra * weight, table, (((spectra.ndim - 1,), (1,)), ((), ())),
        precision=fast, preferred_element_type=jnp.float32,
    )


def parts(packed):
    return (packed[..., :PART], packed[..., PART:])


def conj_times(first, second):
    first_real, first_imag = parts(first)
    second_real, second_imag = parts(second)
    real_part = first_real * second_real + first_imag * second_imag
    imag_part = first_real * second_imag - first_imag * second_real
    return jnp.concatenate([real_part, imag_part], axis=-1)


def product_sum(atom_spec, code_spec):
    atom_real, atom_imag = parts(atom_spec)
    code_real, code_imag = parts(code_spec)
    real_sum = jnp.sum(atom_real * code_real - atom_imag * code_imag, axis=1)
    imag_sum = jnp.sum(atom_real * code_imag + atom_imag * code_real, axis=1)
    return jnp.concatenate([real_sum, imag_sum], axis=-1)


def on_device(images, active, dictionary):
    tiles_here, pixels = images.shape
    tile_count = lax.axis_size("tile")
    atom_count = lax.axis_size("atom")
    table_host, weight_host = half_table()
    table = jnp.asarray(table_host)
    weight = jnp.asarray(weight_host)
    table, weight = lax.optimization_barrier((table, weight))
    width = table.shape[1]

    raw = dictionary.reshape(1, pixels)
    dense = raw.reshape(1, 8, pixels // 8)
    step = lax.all_to_all(jnp.broadcast_to(dense, (tile_count, 8, pixels // 8)), "tile", 0, 0, tiled=True)
    mine = step.reshape(tile_count, pixels)
    own = unit_rows(raw)
    place = lax.axis_index("atom")
    core = place % 2
    chips = atom_count // 2
    chip = place // 2
    other = lax.ppermute(mine, "atom", [(i, i ^ 1) for i in range(atom_count)])
    pair = jnp.concatenate([mine, other])
    pieces = [pair]
    for hop in range(1, chips):
        pieces.append(lax.ppermute(pair, "atom", [(i, ((i // 2 + hop) % chips) * 2 + i % 2) for i in range(atom_count)]))
    every = jnp.concatenate(pieces, axis=0).reshape(atom_count, tile_count, pixels)

    image_spec = forward(images.reshape(1, tiles_here, pixels), table).reshape(tiles_here, width)
    slot_count = tiles_here * ACT
    flat_ids = active.reshape(slot_count)
    where_held = ((chip - flat_ids // 2) % chips) * 2 + (flat_ids % 2 != core).astype(jnp.int32)
    chosen_atoms = jnp.take(every, where_held, axis=0).reshape(slot_count * BLK, pixels)
    norm = jnp.sqrt(jnp.mean(chosen_atoms * chosen_atoms, axis=-1, keepdims=True) + epsilon)
    rows = ACT * BLK
    chosen = (forward(chosen_atoms, table) / norm).reshape(tiles_here, rows, width)
    chosen_real, chosen_imag = parts(chosen)
    power = jnp.sum(chosen_real * chosen_real + chosen_imag * chosen_imag, axis=1)
    bound = jnp.max(power, axis=1) + epsilon
    rate = (1.0 / bound)[:, None, None]
    limit = rate * (shrink_scale * SIDE)
    weights = momentum_weights(ITERS)

    prior = None
    guess = None
    guess_spec = None
    for sweep in range(ITERS):
        if guess is None:
            residual_spec = -image_spec
        else:
            residual_spec = product_sum(chosen, guess_spec) - image_spec
        gradient = inverse(conj_times(chosen, residual_spec[:, None, :]).reshape(tiles_here * rows, width), table, weight)
        gradient = gradient.reshape(tiles_here, rows, pixels)
        if guess is None:
            moved = -(rate * gradient)
        else:
            moved = guess - rate * gradient
        fresh = moved - jnp.clip(moved, -limit, limit)
        if prior is None:
            guess = fresh + weights[sweep] * fresh
        else:
            guess = fresh + weights[sweep] * (fresh - prior)
        prior = fresh
        if sweep + 1 < ITERS:
            guess_spec = forward(guess.reshape(tiles_here * rows, pixels), table).reshape(tiles_here, rows, width)

    code_spec = forward(prior.reshape(tiles_here * rows, pixels), table).reshape(tiles_here, rows, width)
    recon_spec = product_sum(chosen, code_spec)
    residual_spec = recon_spec - image_spec
    slot_terms = conj_times(code_spec, residual_spec[:, None, :]).reshape(slot_count, BLK, width)
    member = (jnp.arange(NBLK, dtype=jnp.int32)[:, None] == flat_ids[None, :]).astype(jnp.float32)
    block_spec = jnp.einsum("bs,skx->bkx", member, slot_terms, precision=fast, preferred_element_type=jnp.float32)
    both = inverse(jnp.concatenate([block_spec.reshape(NBLK * BLK, width), recon_spec], axis=0), table, weight)
    partial = both[:NBLK * BLK].reshape(NBLK, BLK, pixels)
    recon = both[NBLK * BLK:]

    paired = partial.reshape(chips, 2, BLK, pixels)
    keep = lax.dynamic_index_in_dim(paired, core, axis=1, keepdims=False)
    give = lax.dynamic_index_in_dim(paired, 1 - core, axis=1, keepdims=False)
    summed = keep + lax.ppermute(give, "atom", [(i, i ^ 1) for i in range(atom_count)])
    arrived = lax.dynamic_index_in_dim(summed, chip, axis=0, keepdims=False)
    for hop in range(1, chips):
        sent = lax.dynamic_index_in_dim(summed, (chip + hop) % chips, axis=0, keepdims=False)
        arrived = arrived + lax.ppermute(sent, "atom", [(i, ((i // 2 + hop) % chips) * 2 + i % 2) for i in range(atom_count)])
    arrived = arrived.reshape(tile_count, 1, pixels)
    atom_grad = jnp.sum(lax.all_to_all(arrived, "tile", 0, 0, tiled=True), axis=0)

    scale = jnp.sqrt(jnp.mean(atom_grad * atom_grad, axis=-1, keepdims=True) + epsilon)
    atoms = unit_rows(own - step_ratio * atom_grad / scale)
    return (recon, atoms.reshape(dictionary.shape))


def solution(mesh):
    in_specs = (P(("tile", "atom"), None), P(("tile", "atom"), None), P("atom", "tile", None))
    out_specs = (P(("tile", "atom"), None), P("atom", "tile", None))
    return jax.shard_map(
        on_device, mesh=mesh, in_specs=in_specs, out_specs=out_specs, check_vma=False
    )
```
